256 devices in a mesh: path: 64 (over z, x, core), rep: 4 (over y).
Axes of the slice: x: 4, y: 4, z: 8, core: 2. Of those that a mesh axis runs over, the one named last changes fastest.
Arguments:
- start_state: float32 [32, 65536], P(None, 'path'), may hold values from -1.8 to 1.8
- increments: float32 [2, 32, 65536], P(None, None, 'path'), may hold values from -6 to 6
- vol_factor: float32 [32, 32], replicated, may hold values from -0.3 to 0.3
- quad_dirs: float32 [223, 32], replicated, may hold values from -1.5 to 1.5
- bundle_ids: int32 [2, 65536, 1], P(None, 'path'), may hold values from 0 to 255; in each aligned block of 1024 rows (0 to 1023, 1024 to 2047, ..., all dimensions but the last counted through in order) at most 8 rows name the same one
- bundle_slot: int32 [256], replicated, may hold values from 0 to 255, each once
Outputs:
- values: float32 [2, 65536], P(None, 'path')
- coefficients: float32 [2, 256, 256], P(None, 'path', 'rep')
The draws below stay inside these ranges and needn't reach their ends.
Inputs may be any that keep to these rules, and one draw needn't show every extreme that they name: `bundle_ids`: at each date, no bundle id appears more than 8 times among the paths of one device; in every draw some device holds exactly 8 paths of one bundle. A permutation: bundle b sits at slot bundle_slot[b], and slot s belongs to the owner s // 4 along path.
All inputs are finite; a program needn't handle non-finite values.
Results may differ from the reference program's by a relative error of at most 0.0003.
Values sent between devices are 32-bit elements; how exact they have to be, the bound alone decides.
No kernel may reach another device: no remote copies, remote signals or barrier semaphores. Data moves between devices by JAX's collectives and lax.ppermute only.
A program may use at most 64 MiB of HBM per device.

```python
import math
import jax
import jax.numpy as jnp
import numpy as np
from jax import lax

ASSETS = 32
BASIS = 256
QUAD = 223
DATES = 2
PATH_DEV = 1024
BUNDLES = 256
PATHS = 65536
MOST = 8
N_PATH = 64


def levels(stream_key, dims, cuts, smallest, top_value):
    loudness = 1.0
    for position, parts in cuts:
        draws = jax.random.uniform(jax.random.fold_in(jax.random.fold_in(stream_key, 6), position), (parts,), jnp.float32, smallest / len(cuts), top_value / len(cuts))
        loudness = loudness * jnp.repeat(jnp.exp(draws), dims[position] // parts).reshape((-1,) + (1,) * (len(dims) - 1 - position))
    return loudness


def deal_out(own_key, own, number, rows, count, top, most, skew):
    sequence = jax.random.permutation(own_key, count)
    packed, ordinary = portions_of(count, rows * top, most, skew, True), portions_of(count, rows * top, most, skew, False)
    places = jnp.arange(count)

    def named(tallies, offset_by):
        used = int((tallies > 0).sum())
        fixed = max(1, used // 4)
        moved = fixed + (places - fixed + offset_by * (used - fixed)) % max(1, count - fixed)
        return jnp.zeros((count,), jnp.int32).at[sequence[jnp.where(places < fixed, places, moved)]].set(jnp.asarray(tallies, jnp.int32))

    tallies = jnp.where(number % 4 == 0, named(packed, number // 4), named(ordinary, number - number // 4 - 1))
    mixed = jax.random.permutation(jax.random.fold_in(own, 3), count)
    donor, taker = mixed[0:count // 2 * 2:2], mixed[1:count // 2 * 2:2]
    room = jnp.minimum(tallies[donor] - 1, most - tallies[taker]) // 2
    room = jnp.where((donor == sequence[0]) | (taker == sequence[0]) | (tallies[taker] == 0), 0, jnp.maximum(room, 0))
    moved = jax.random.randint(jax.random.fold_in(own, 4), (count // 2,), 0, 1 << 20) % (room + 1)
    tallies = tallies.at[donor].add(-moved).at[taker].add(moved)
    items = jnp.searchsorted(jnp.cumsum(tallies), jnp.arange(rows * top), side="right").astype(jnp.int32)
    grid = items.reshape(top, rows).T
    grid = grid[jax.random.permutation(jax.random.fold_in(own, 1), rows)]
    offset_by = jax.random.randint(jax.random.fold_in(own, 2), (rows, 1), 0, top)
    return jnp.take_along_axis(grid, (jnp.arange(top)[None, :] + offset_by) % top, axis=1)


def portions_of(count, total, bound, slope, full):
    portions = [(1 << 20) // math.isqrt(grade ** slope) + 1 for grade in range(1, count + 1)]
    largest = bound if full else min(bound, max(-(-total // count), total * portions[0] // sum(portions)))
    least = 1 if total - largest >= count - 1 else 0
    holding, spare = [largest] + [least] * (count - 1), total - largest - least * (count - 1)
    while spare > 0:
        free = [i for i in range(1, count) if holding[i] < largest] or [i for i in range(1, count) if holding[i] < bound]
        pool, left = sum([portions[i] for i in free]), spare
        for i in free:
            extra = min(bound - holding[i], max(1, left * portions[i] // pool), spare)
            holding[i] = holding[i] + extra
            spare = spare - extra
    return np.array(holding)


def bell_draw(rng, shape, deviation, limit, split=(), kind=jnp.bfloat16):
    array = deviation * jax.random.normal(rng, shape, jnp.float32)
    if split:
        array = array * levels(rng, shape, split, -0.22, 0.18)
    return jnp.clip(array, -limit, limit).astype(kind)


def setup_inputs(seed: int = 0) -> dict:
    splits = jax.random.split(jax.random.key(seed), 7)
    start_state = bell_draw(splits[0], (ASSETS, PATHS), 0.3, 1.8, ((1, 64),), jnp.float32)
    increments = bell_draw(splits[1], (DATES, ASSETS, PATHS), 1.0, 6.0, ((2, 64),), jnp.float32)
    vol_factor = bell_draw(splits[2], (ASSETS, ASSETS), 0.06, 0.3, (), jnp.float32)
    quad_dirs = bell_draw(splits[3], (QUAD, ASSETS), 0.3, 1.5, (), jnp.float32)
    bundle_ids_keys = jax.random.split(jax.random.fold_in(splits[4], 1), DATES * PATHS // PATH_DEV)
    bundle_ids_turns = jax.random.permutation(jax.random.fold_in(splits[4], 3), DATES * PATHS // PATH_DEV)
    bundle_ids = jax.vmap(lambda own, number: deal_out(jax.random.fold_in(splits[4], 2), own, number, PATH_DEV, BUNDLES, 1, MOST, 2))(bundle_ids_keys, bundle_ids_turns).reshape((DATES, PATHS, 1))
    bundle_slot = jax.random.permutation(splits[5], BUNDLES).astype(jnp.int32)
    return {"start_state": start_state, "increments": increments, "vol_factor": vol_factor, "quad_dirs": quad_dirs, "bundle_ids": bundle_ids, "bundle_slot": bundle_slot}


RIDGE_TERM = 32.0
DISCOUNT = 0.97
NOTIONAL = 10.0
HIGHEST = lax.Precision.HIGHEST

def basis_features(states, quad_dirs):
    projected = jnp.dot(quad_dirs.astype(jnp.float32), states.astype(jnp.float32), precision=HIGHEST, preferred_element_type=jnp.float32)
    constant = jnp.ones((1, states.shape[1]), jnp.float32)
    return jnp.concatenate([constant, states, projected * projected], axis=0)

def moment_features(states, quad_dirs, offsets):
    projected = jnp.dot(quad_dirs.astype(jnp.float32), states.astype(jnp.float32), precision=HIGHEST, preferred_element_type=jnp.float32)
    constant = jnp.ones((1, states.shape[1]), jnp.float32)
    return jnp.concatenate([constant, states, projected * projected + offsets[:, None]], axis=0)

def exercise_value(states):
    return NOTIONAL * jnp.maximum(jnp.mean(jnp.exp(states), axis=0) - 1.0, 0.0)

def regression(bundle_of, states, values, quad_dirs):
    capacity = N_PATH * MOST
    ranking = jnp.argsort(bundle_of, stable=True)
    ordered = jnp.take(bundle_of, ranking)
    labels = jnp.arange(BUNDLES, dtype=jnp.int32)
    starts = jnp.searchsorted(ordered, labels, side='left').astype(jnp.int32)
    counts = jnp.searchsorted(ordered, labels, side='right').astype(jnp.int32) - starts
    padded_states = jnp.concatenate([jnp.take(states, ranking, axis=1), jnp.zeros((ASSETS, capacity), jnp.float32)], axis=1)
    padded_values = jnp.concatenate([jnp.take(values, ranking), jnp.zeros((capacity,), jnp.float32)])
    identity = jnp.eye(BASIS, dtype=jnp.float32)

    def solve_bundle(label):
        begin = starts[label]
        rows_states = lax.dynamic_slice_in_dim(padded_states, begin, capacity, 1)
        rows_values = lax.dynamic_slice_in_dim(padded_values, begin, capacity, 0)
        present = (jnp.arange(capacity, dtype=jnp.int32) < counts[label]).astype(jnp.float32)
        features = basis_features(rows_states, quad_dirs) * present[None, :]
        gram_matrix = jnp.dot(features, features.T, precision=HIGHEST) + RIDGE_TERM * identity
        right_side = jnp.dot(features, rows_values * present, precision=HIGHEST)
        factor = jnp.linalg.cholesky(gram_matrix)
        halfway = lax.linalg.triangular_solve(factor, right_side[:, None], left_side=True, lower=True)
        solved = lax.linalg.triangular_solve(factor, halfway, left_side=True, lower=True, transpose_a=True)
        return solved[:, 0]
    return lax.map(solve_bundle, labels)

def continuation(weights, bundle_of, states, quad_dirs, offsets):
    block_bundles = bundle_of.reshape(N_PATH, PATH_DEV)
    block_states = jnp.transpose(states.reshape(ASSETS, N_PATH, PATH_DEV), (1, 0, 2))

    def one_block(pieces):
        bundles_here, states_here = pieces
        moments = moment_features(states_here, quad_dirs, offsets)
        picked = jnp.take(weights, bundles_here, axis=0)
        return jnp.sum(picked.T * moments, axis=0)
    return lax.map(one_block, (block_bundles, block_states)).reshape(N_PATH * PATH_DEV)

def backward_date(bundle_of, state_now, state_next, value_next, quad_dirs, offsets):
    weights = regression(bundle_of, state_next, value_next, quad_dirs)
    carried = continuation(weights, bundle_of, state_now, quad_dirs, offsets)
    return (jnp.maximum(exercise_value(state_now), DISCOUNT * carried), weights)

def reference(start_state, increments, vol_factor, quad_dirs, bundle_ids, bundle_slot):
    middle = start_state + jnp.dot(vol_factor.astype(jnp.float32), increments[0].astype(jnp.float32), precision=HIGHEST, preferred_element_type=jnp.float32)
    final = middle + jnp.dot(vol_factor.astype(jnp.float32), increments[1].astype(jnp.float32), precision=HIGHEST, preferred_element_type=jnp.float32)
    mixed = jnp.dot(quad_dirs.astype(jnp.float32), vol_factor.astype(jnp.float32), precision=HIGHEST, preferred_element_type=jnp.float32)
    offsets = jnp.sum(mixed * mixed, axis=1)
    value_final = exercise_value(final)
    value_middle, weights_middle = backward_date(bundle_ids[0, :, 0], middle, final, value_final, quad_dirs, offsets)
    value_start, weights_start = backward_date(bundle_ids[1, :, 0], start_state, middle, value_middle, quad_dirs, offsets)
    values = jnp.stack([value_middle, value_start])
    slot_middle = jnp.zeros_like(weights_middle).at[bundle_slot].set(weights_middle)
    slot_start = jnp.zeros_like(weights_start).at[bundle_slot].set(weights_start)
    return (values, jnp.stack([slot_middle, slot_start]))
```

```python
import jax
import jax.numpy as jnp
from jax import lax
from jax.sharding import PartitionSpec as P

BASIS = 256
MOST = 8

RIDGE_TERM = 32.0
DISCOUNT = 0.97
NOTIONAL = 10.0
HIGHEST = lax.Precision.HIGHEST


def exercise_value(states):
    return NOTIONAL * jnp.maximum(jnp.mean(jnp.exp(states), axis=0) - 1.0, 0.0)


def exercise_rows(states):
    return NOTIONAL * jnp.maximum(jnp.mean(jnp.exp(states), axis=1) - 1.0, 0.0)


def routing(bundle_of, bundle_slot, rep_index, reps):
    path_count = bundle_of.shape[0]
    bundles = bundle_slot.shape[0]
    labels = lax.broadcasted_iota(jnp.int32, (path_count, bundles), 1)
    slot_of = jnp.sum(jnp.where(bundle_of[:, None] == labels, bundle_slot[None, :], 0), axis=1)
    owners = bundles // reps
    later = lax.broadcasted_iota(jnp.int32, (path_count, path_count), 0)
    earlier = lax.broadcasted_iota(jnp.int32, (path_count, path_count), 1)
    same = (slot_of[:, None] == slot_of[None, :]) & (earlier < later)
    rank = jnp.sum(same.astype(jnp.int32), axis=1)
    mine = (slot_of % reps) == rep_index
    position = jnp.where(mine, (slot_of // reps) * MOST + rank, -1)
    places = lax.broadcasted_iota(jnp.int32, (owners * MOST, path_count), 0)
    return (places == position[None, :]).astype(jnp.float32)


def send_rows(onehot, rows):
    return lax.dot_general(onehot, rows, (((1,), (1,)), ((), ())), precision=HIGHEST,
                           preferred_element_type=jnp.float32)


def exchange(block, owners):
    shaped = block.reshape((owners, MOST) + block.shape[1:])
    arrived = lax.all_to_all(shaped, "path", 0, 0, tiled=True)
    return arrived.reshape(block.shape)


def features_of(present, states, quad_dirs):
    projected = lax.dot_general(states, quad_dirs, (((1,), (1,)), ((), ())), precision=HIGHEST,
                                preferred_element_type=jnp.float32)
    return jnp.concatenate([present, states, projected * projected], axis=1)


def moments_of(states, quad_dirs, offsets):
    projected = lax.dot_general(states, quad_dirs, (((1,), (1,)), ((), ())), precision=HIGHEST,
                                preferred_element_type=jnp.float32)
    constant = jnp.ones((states.shape[0], 1), jnp.float32)
    return jnp.concatenate([constant, states, projected * projected + offsets[None, :]], axis=1)


def factor_gram(features):
    gram = lax.dot_general(features, features, (((0,), (0,)), ((), ())), precision=HIGHEST,
                           preferred_element_type=jnp.float32)
    gram = gram + RIDGE_TERM * jnp.eye(BASIS, dtype=jnp.float32)
    return jnp.linalg.cholesky(gram)


def solve_weights(factor, features, values):
    right_side = lax.dot_general(features, values, (((0,), (0,)), ((), ())), precision=HIGHEST,
                                 preferred_element_type=jnp.float32)
    halfway = lax.linalg.triangular_solve(factor, right_side[:, None], left_side=True, lower=True)
    weights = lax.linalg.triangular_solve(factor, halfway, left_side=True, lower=True, transpose_a=True)
    return weights[:, 0]


def new_values(weights, current, quad_dirs, offsets):
    moments = moments_of(current, quad_dirs, offsets)
    carried = jnp.dot(moments, weights, precision=HIGHEST, preferred_element_type=jnp.float32)
    return jnp.maximum(exercise_rows(current), DISCOUNT * carried)


def go_home(onehot, owner_values, owners):
    back = exchange(owner_values, owners)
    local = jnp.dot(back, onehot, precision=HIGHEST, preferred_element_type=jnp.float32)
    return lax.psum(local, "rep")


def coefficient_block(weights, reps):
    shaped = weights.reshape(reps, BASIS // reps)
    return lax.all_to_all(shaped, "rep", 0, 0, tiled=True)


def body(start_state, increments, vol_factor, quad_dirs, bundle_ids, bundle_slot):
    reps = lax.axis_size("rep")
    owners = bundle_slot.shape[0] // reps
    rep_index = lax.axis_index("rep")
    middle = start_state + jnp.dot(
        vol_factor, increments[0], precision=HIGHEST, preferred_element_type=jnp.float32
    )
    final = middle + jnp.dot(
        vol_factor, increments[1], precision=HIGHEST, preferred_element_type=jnp.float32
    )
    mixed = jnp.dot(quad_dirs, vol_factor, precision=HIGHEST, preferred_element_type=jnp.float32)
    offsets = jnp.sum(mixed * mixed, axis=1)
    assets = start_state.shape[0]
    ones = jnp.ones((1, start_state.shape[1]), jnp.float32)

    late_map = routing(bundle_ids[0, :, 0], bundle_slot, rep_index, reps)
    early_map = routing(bundle_ids[1, :, 0], bundle_slot, rep_index, reps)

    late_rows = exchange(send_rows(late_map, jnp.concatenate([ones, middle, final], axis=0)), owners)
    early_rows = exchange(send_rows(early_map, jnp.concatenate([ones, start_state, middle], axis=0)), owners)

    present = late_rows[:, :1]
    current = late_rows[:, 1:1 + assets]
    following = late_rows[:, 1 + assets:]
    late_features = features_of(present, following, quad_dirs)
    late_factor = factor_gram(late_features)
    late_weights = solve_weights(late_factor, late_features, exercise_rows(following))
    late_owner_values = new_values(late_weights, current, quad_dirs, offsets)
    value_middle = go_home(late_map, late_owner_values, owners)

    present = early_rows[:, :1]
    current = early_rows[:, 1:1 + assets]
    following = early_rows[:, 1 + assets:]
    early_features = features_of(present, following, quad_dirs)
    early_factor = factor_gram(early_features)
    early_targets = exchange(send_rows(early_map, value_middle[None, :]), owners)[:, 0]
    early_weights = solve_weights(early_factor, early_features, early_targets)
    early_owner_values = new_values(early_weights, current, quad_dirs, offsets)
    value_start = go_home(early_map, early_owner_values, owners)

    coefficients = jnp.stack(
        [coefficient_block(late_weights, reps), coefficient_block(early_weights, reps)]
    )
    return (jnp.stack([value_middle, value_start]), coefficients)


def solution(mesh):
    placed = (P(None, "path"), P(None, None, "path"), P(), P(), P(None, "path", None), P())
    return jax.shard_map(
        body,
        mesh=mesh,
        in_specs=placed,
        out_specs=(P(None, "path"), P(None, "path", "rep")),
        check_vma=False,
    )
```

```python
import jax
import jax.numpy as jnp
from jax import lax
from jax.sharding import PartitionSpec as P

BASIS = 256
MOST = 8

RIDGE_TERM = 32.0
DISCOUNT = 0.97
NOTIONAL = 10.0
HIGHEST = lax.Precision.HIGHEST


def exercise_value(states):
    return NOTIONAL * jnp.maximum(jnp.mean(jnp.exp(states), axis=0) - 1.0, 0.0)


def exercise_rows(states):
    return NOTIONAL * jnp.maximum(jnp.mean(jnp.exp(states), axis=1) - 1.0, 0.0)


def routing(bundle_of, bundle_slot, rep_index, reps):
    path_count = bundle_of.shape[0]
    bundles = bundle_slot.shape[0]
    labels = lax.broadcasted_iota(jnp.int32, (path_count, bundles), 1)
    slot_of = jnp.sum(jnp.where(bundle_of[:, None] == labels, bundle_slot[None, :], 0), axis=1)
    owners = bundles // reps
    later = lax.broadcasted_iota(jnp.int32, (path_count, path_count), 0)
    earlier = lax.broadcasted_iota(jnp.int32, (path_count, path_count), 1)
    same = (slot_of[:, None] == slot_of[None, :]) & (earlier < later)
    rank = jnp.sum(same.astype(jnp.int32), axis=1)
    mine = (slot_of % reps) == rep_index
    position = jnp.where(mine, (slot_of // reps) * MOST + rank, -1)
    places = lax.broadcasted_iota(jnp.int32, (owners * MOST, path_count), 0)
    forward = (places == position[None, :]).astype(jnp.float32)
    slot_rows = lax.broadcasted_iota(jnp.int32, (bundles, path_count), 0)
    slots = (slot_rows == slot_of[None, :]).astype(jnp.float32)
    return forward, slots, rank


def send_rows(onehot, rows):
    return lax.dot_general(onehot, rows, (((1,), (1,)), ((), ())), precision=HIGHEST,
                           preferred_element_type=jnp.float32)


def exchange(block, owners):
    shaped = block.reshape((owners, MOST) + block.shape[1:])
    arrived = lax.all_to_all(shaped, "path", 0, 0, tiled=True)
    return arrived.reshape(block.shape)


def features_of(present, states, quad_dirs):
    projected = lax.dot_general(states, quad_dirs, (((1,), (1,)), ((), ())), precision=HIGHEST,
                                preferred_element_type=jnp.float32)
    return jnp.concatenate([present, states, projected * projected], axis=1)


def moments_of(states, quad_dirs, offsets):
    projected = lax.dot_general(states, quad_dirs, (((1,), (1,)), ((), ())), precision=HIGHEST,
                                preferred_element_type=jnp.float32)
    constant = jnp.ones((states.shape[0], 1), jnp.float32)
    return jnp.concatenate([constant, states, projected * projected + offsets[None, :]], axis=1)


def factor_gram(features):
    gram = lax.dot_general(features, features, (((0,), (0,)), ((), ())), precision=HIGHEST,
                           preferred_element_type=jnp.float32)
    gram = gram + RIDGE_TERM * jnp.eye(BASIS, dtype=jnp.float32)
    return jnp.linalg.cholesky(gram)


def solve_weights(factor, features, values):
    right_side = lax.dot_general(features, values, (((0,), (0,)), ((), ())), precision=HIGHEST,
                                 preferred_element_type=jnp.float32)
    halfway = lax.linalg.triangular_solve(factor, right_side[:, None], left_side=True, lower=True)
    weights = lax.linalg.triangular_solve(factor, halfway, left_side=True, lower=True, transpose_a=True)
    return weights[:, 0]


def new_values(weights, current, quad_dirs, offsets):
    moments = moments_of(current, quad_dirs, offsets)
    carried = jnp.dot(moments, weights, precision=HIGHEST, preferred_element_type=jnp.float32)
    return jnp.maximum(exercise_rows(current), DISCOUNT * carried)


def go_home(owner_values, weights, slots, rank, owners, reps):
    width = BASIS // reps
    per_home = jnp.broadcast_to(owner_values.reshape(owners, 1, MOST), (owners, reps, MOST))
    blocks = jnp.broadcast_to(weights.reshape(1, reps, width), (owners, reps, width))
    message = jnp.concatenate([per_home, blocks], axis=2).reshape(owners * reps, MOST + width)
    arrived = lax.all_to_all(message, ("path", "rep"), 0, 0, tiled=True)
    by_slot = arrived[:, :MOST]
    picked = lax.dot_general(by_slot, slots, (((0,), (0,)), ((), ())), precision=HIGHEST,
                             preferred_element_type=jnp.float32)
    ranks = lax.broadcasted_iota(jnp.int32, picked.shape, 0)
    values = jnp.sum(jnp.where(ranks == rank[None, :], picked, 0.0), axis=0)
    mine = lax.dynamic_index_in_dim(arrived.reshape(owners, reps, MOST + width), lax.axis_index("path"), 0, False)
    return values, mine[:, MOST:]


def body(start_state, increments, vol_factor, quad_dirs, bundle_ids, bundle_slot):
    reps = lax.axis_size("rep")
    owners = bundle_slot.shape[0] // reps
    rep_index = lax.axis_index("rep")
    middle = start_state + jnp.dot(
        vol_factor, increments[0], precision=HIGHEST, preferred_element_type=jnp.float32
    )
    final = middle + jnp.dot(
        vol_factor, increments[1], precision=HIGHEST, preferred_element_type=jnp.float32
    )
    mixed = jnp.dot(quad_dirs, vol_factor, precision=HIGHEST, preferred_element_type=jnp.float32)
    offsets = jnp.sum(mixed * mixed, axis=1)
    assets = start_state.shape[0]
    ones = jnp.ones((1, start_state.shape[1]), jnp.float32)

    late_map, late_slots, late_rank = routing(bundle_ids[0, :, 0], bundle_slot, rep_index, reps)
    early_map, early_slots, early_rank = routing(bundle_ids[1, :, 0], bundle_slot, rep_index, reps)

    outgoing = jnp.concatenate(
        [send_rows(late_map, jnp.concatenate([ones, middle, final], axis=0)),
         send_rows(early_map, jnp.concatenate([ones, start_state, middle], axis=0))], axis=1)
    arrived = exchange(outgoing, owners)
    width = 1 + 2 * assets

    late_rows = arrived[:, :width]
    present = late_rows[:, :1]
    current = late_rows[:, 1:1 + assets]
    following = late_rows[:, 1 + assets:]
    late_features = features_of(present, following, quad_dirs)
    late_factor = factor_gram(late_features)
    late_weights = solve_weights(late_factor, late_features, exercise_rows(following))
    late_owner_values = new_values(late_weights, current, quad_dirs, offsets)
    value_middle, late_block = go_home(late_owner_values, late_weights, late_slots, late_rank, owners, reps)

    early_rows = arrived[:, width:]
    present = early_rows[:, :1]
    current = early_rows[:, 1:1 + assets]
    following = early_rows[:, 1 + assets:]
    early_features = features_of(present, following, quad_dirs)
    early_factor = factor_gram(early_features)
    sent_values = lax.dot_general(value_middle[None, :], early_map, (((1,), (1,)), ((), ())), precision=HIGHEST,
                                  preferred_element_type=jnp.float32)
    early_targets = exchange(sent_values.reshape(-1), owners)
    early_weights = solve_weights(early_factor, early_features, early_targets)
    early_owner_values = new_values(early_weights, current, quad_dirs, offsets)
    value_start, early_block = go_home(early_owner_values, early_weights, early_slots, early_rank, owners, reps)

    return (jnp.stack([value_middle, value_start]), jnp.stack([late_block, early_block]))


def solution(mesh):
    placed = (P(None, "path"), P(None, None, "path"), P(), P(), P(None, "path", None), P())
    return jax.shard_map(
        body,
        mesh=mesh,
        in_specs=placed,
        out_specs=(P(None, "path"), P(None, "path", "rep")),
        check_vma=False,
    )
```

```python
import jax
import jax.numpy as jnp
from jax import lax
from jax.sharding import PartitionSpec as P

BASIS = 256
MOST = 8

RIDGE_TERM = 32.0
DISCOUNT = 0.97
NOTIONAL = 10.0
HIGHEST = lax.Precision.HIGHEST


def exercise_value(states):
    return NOTIONAL * jnp.maximum(jnp.mean(jnp.exp(states), axis=0) - 1.0, 0.0)


def exercise_rows(states):
    return NOTIONAL * jnp.maximum(jnp.mean(jnp.exp(states), axis=1) - 1.0, 0.0)


def routing(bundle_of, bundle_slot, rep_index, reps):
    path_count = bundle_of.shape[0]
    bundles = bundle_slot.shape[0]
    labels = lax.broadcasted_iota(jnp.int32, (path_count, bundles), 1)
    slot_of = jnp.sum(jnp.where(bundle_of[:, None] == labels, bundle_slot[None, :], 0), axis=1)
    owners = bundles // reps
    later = lax.broadcasted_iota(jnp.int32, (path_count, path_count), 0)
    earlier = lax.broadcasted_iota(jnp.int32, (path_count, path_count), 1)
    same = (slot_of[:, None] == slot_of[None, :]) & (earlier < later)
    rank = jnp.sum(same.astype(jnp.int32), axis=1)
    mine = (slot_of % reps) == rep_index
    position = jnp.where(mine, (slot_of // reps) * MOST + rank, -1)
    places = lax.broadcasted_iota(jnp.int32, (owners * MOST, path_count), 0)
    forward = (places == position[None, :]).astype(jnp.float32)
    slot_rows = lax.broadcasted_iota(jnp.int32, (bundles, path_count), 0)
    slots = (slot_rows == slot_of[None, :]).astype(jnp.float32)
    return forward, slots, rank


def send_rows(onehot, rows):
    return lax.dot_general(onehot, rows, (((1,), (1,)), ((), ())), precision=HIGHEST,
                           preferred_element_type=jnp.float32)


def exchange(block, owners):
    shaped = block.reshape((owners, MOST) + block.shape[1:])
    arrived = lax.all_to_all(shaped, "path", 0, 0, tiled=True)
    return arrived.reshape(block.shape)


def features_of(present, states, quad_dirs):
    projected = lax.dot_general(states, quad_dirs, (((1,), (1,)), ((), ())), precision=HIGHEST,
                                preferred_element_type=jnp.float32)
    return jnp.concatenate([present, states, projected * projected], axis=1)


def moments_of(states, quad_dirs, offsets):
    projected = lax.dot_general(states, quad_dirs, (((1,), (1,)), ((), ())), precision=HIGHEST,
                                preferred_element_type=jnp.float32)
    constant = jnp.ones((states.shape[0], 1), jnp.float32)
    return jnp.concatenate([constant, states, projected * projected + offsets[None, :]], axis=1)


def factor_gram(features):
    gram = lax.dot_general(features, features, (((0,), (0,)), ((), ())), precision=HIGHEST,
                           preferred_element_type=jnp.float32)
    gram = gram + RIDGE_TERM * jnp.eye(BASIS, dtype=jnp.float32)
    half = BASIS // 2
    identity = jnp.eye(half, dtype=jnp.float32)
    upper_factor = jnp.linalg.cholesky(gram[:half, :half])
    upper_inverse = lax.linalg.triangular_solve(upper_factor, identity, left_side=True, lower=True)
    below = lax.dot_general(gram[half:, :half], upper_inverse, (((1,), (1,)), ((), ())), precision=HIGHEST,
                            preferred_element_type=jnp.float32)
    rest = gram[half:, half:] - lax.dot_general(below, below, (((1,), (1,)), ((), ())), precision=HIGHEST,
                                                preferred_element_type=jnp.float32)
    lower_factor = jnp.linalg.cholesky(rest)
    lower_inverse = lax.linalg.triangular_solve(lower_factor, identity, left_side=True, lower=True)
    return upper_inverse, below, lower_inverse


def matvec(matrix, vector, transpose=False):
    dims = (((0,), (0,)), ((), ())) if transpose else (((1,), (0,)), ((), ()))
    return lax.dot_general(matrix, vector, dims, precision=HIGHEST, preferred_element_type=jnp.float32)


def solve_weights(factor, features, values):
    upper_inverse, below, lower_inverse = factor
    half = BASIS // 2
    right_side = lax.dot_general(features, values, (((0,), (0,)), ((), ())), precision=HIGHEST,
                                 preferred_element_type=jnp.float32)
    first = matvec(upper_inverse, right_side[:half])
    second = matvec(lower_inverse, right_side[half:] - matvec(below, first))
    second = matvec(lower_inverse, second, transpose=True)
    first = matvec(upper_inverse, first - matvec(below, second, transpose=True), transpose=True)
    return jnp.concatenate([first, second])


def new_values(weights, current, quad_dirs, offsets):
    moments = moments_of(current, quad_dirs, offsets)
    carried = jnp.dot(moments, weights, precision=HIGHEST, preferred_element_type=jnp.float32)
    return jnp.maximum(exercise_rows(current), DISCOUNT * carried)


def go_home(owner_values, weights, slots, rank, owners, reps):
    width = BASIS // reps
    per_home = jnp.broadcast_to(owner_values.reshape(owners, 1, MOST), (owners, reps, MOST))
    blocks = jnp.broadcast_to(weights.reshape(1, reps, width), (owners, reps, width))
    message = jnp.concatenate([per_home, blocks], axis=2).reshape(owners * reps, MOST + width)
    arrived = lax.all_to_all(message, ("path", "rep"), 0, 0, tiled=True)
    by_slot = arrived[:, :MOST]
    picked = lax.dot_general(by_slot, slots, (((0,), (0,)), ((), ())), precision=HIGHEST,
                             preferred_element_type=jnp.float32)
    ranks = lax.broadcasted_iota(jnp.int32, picked.shape, 0)
    values = jnp.sum(jnp.where(ranks == rank[None, :], picked, 0.0), axis=0)
    mine = lax.dynamic_index_in_dim(arrived.reshape(owners, reps, MOST + width), lax.axis_index("path"), 0, False)
    return values, mine[:, MOST:]


def body(start_state, increments, vol_factor, quad_dirs, bundle_ids, bundle_slot):
    reps = lax.axis_size("rep")
    owners = bundle_slot.shape[0] // reps
    rep_index = lax.axis_index("rep")
    middle = start_state + jnp.dot(
        vol_factor, increments[0], precision=HIGHEST, preferred_element_type=jnp.float32
    )
    final = middle + jnp.dot(
        vol_factor, increments[1], precision=HIGHEST, preferred_element_type=jnp.float32
    )
    mixed = jnp.dot(quad_dirs, vol_factor, precision=HIGHEST, preferred_element_type=jnp.float32)
    offsets = jnp.sum(mixed * mixed, axis=1)
    assets = start_state.shape[0]
    ones = jnp.ones((1, start_state.shape[1]), jnp.float32)

    late_map, late_slots, late_rank = routing(bundle_ids[0, :, 0], bundle_slot, rep_index, reps)
    early_map, early_slots, early_rank = routing(bundle_ids[1, :, 0], bundle_slot, rep_index, reps)

    outgoing = jnp.concatenate(
        [send_rows(late_map, jnp.concatenate([ones, middle, final], axis=0)),
         send_rows(early_map, jnp.concatenate([ones, start_state, middle], axis=0))], axis=1)
    arrived = exchange(outgoing, owners)
    width = 1 + 2 * assets

    late_rows = arrived[:, :width]
    present = late_rows[:, :1]
    current = late_rows[:, 1:1 + assets]
    following = late_rows[:, 1 + assets:]
    late_features = features_of(present, following, quad_dirs)
    late_factor = factor_gram(late_features)
    late_weights = solve_weights(late_factor, late_features, exercise_rows(following))
    late_owner_values = new_values(late_weights, current, quad_dirs, offsets)
    value_middle, late_block = go_home(late_owner_values, late_weights, late_slots, late_rank, owners, reps)

    early_rows = arrived[:, width:]
    present = early_rows[:, :1]
    current = early_rows[:, 1:1 + assets]
    following = early_rows[:, 1 + assets:]
    early_features = features_of(present, following, quad_dirs)
    early_factor = factor_gram(early_features)
    sent_values = jnp.sum(early_map * value_middle[None, :], axis=1)
    early_targets = exchange(sent_values, owners)
    early_weights = solve_weights(early_factor, early_features, early_targets)
    early_owner_values = new_values(early_weights, current, quad_dirs, offsets)
    value_start, early_block = go_home(early_owner_values, early_weights, early_slots, early_rank, owners, reps)

    return (jnp.stack([value_middle, value_start]), jnp.stack([late_block, early_block]))


def solution(mesh):
    placed = (P(None, "path"), P(None, None, "path"), P(), P(), P(None, "path", None), P())
    return jax.shard_map(
        body,
        mesh=mesh,
        in_specs=placed,
        out_specs=(P(None, "path"), P(None, "path", "rep")),
        check_vma=False,
    )
```

```python
import jax
import jax.numpy as jnp
from jax import lax
from jax.sharding import PartitionSpec as P

BASIS = 256
MOST = 8

RIDGE_TERM = 32.0
DISCOUNT = 0.97
NOTIONAL = 10.0
HIGHEST = lax.Precision.HIGHEST


def exercise_value(states):
    return NOTIONAL * jnp.maximum(jnp.mean(jnp.exp(states), axis=0) - 1.0, 0.0)


def exercise_rows(states):
    return NOTIONAL * jnp.maximum(jnp.mean(jnp.exp(states), axis=1) - 1.0, 0.0)


def routing(bundle_of, bundle_slot, rep_index, reps):
    path_count = bundle_of.shape[0]
    bundles = bundle_slot.shape[0]
    labels = lax.broadcasted_iota(jnp.int32, (path_count, bundles), 1)
    slot_of = jnp.sum(jnp.where(bundle_of[:, None] == labels, bundle_slot[None, :], 0), axis=1)
    owners = bundles // reps
    later = lax.broadcasted_iota(jnp.int32, (path_count, path_count), 0)
    earlier = lax.broadcasted_iota(jnp.int32, (path_count, path_count), 1)
    same = (slot_of[:, None] == slot_of[None, :]) & (earlier < later)
    rank = jnp.sum(same.astype(jnp.int32), axis=1)
    mine = (slot_of % reps) == rep_index
    position = jnp.where(mine, (slot_of // reps) * MOST + rank, -1)
    places = lax.broadcasted_iota(jnp.int32, (owners * MOST, path_count), 0)
    forward = (places == position[None, :]).astype(jnp.float32)
    slot_rows = lax.broadcasted_iota(jnp.int32, (bundles, path_count), 0)
    slots = (slot_rows == slot_of[None, :]).astype(jnp.float32)
    return forward, slots, rank, slot_of


def send_rows(onehot, rows):
    return lax.dot_general(onehot, rows, (((1,), (1,)), ((), ())), precision=HIGHEST,
                           preferred_element_type=jnp.float32)


def exchange(block, owners):
    shaped = block.reshape((owners, MOST) + block.shape[1:])
    arrived = lax.all_to_all(shaped, "path", 0, 0, tiled=True)
    return arrived.reshape(block.shape)


def features_of(present, states, quad_dirs):
    projected = lax.dot_general(states, quad_dirs, (((1,), (1,)), ((), ())), precision=HIGHEST,
                                preferred_element_type=jnp.float32)
    return jnp.concatenate([present, states, projected * projected], axis=1)


def moments_of(states, quad_dirs, offsets):
    projected = lax.dot_general(states, quad_dirs, (((1,), (1,)), ((), ())), precision=HIGHEST,
                                preferred_element_type=jnp.float32)
    constant = jnp.ones((states.shape[0], 1), jnp.float32)
    return jnp.concatenate([constant, states, projected * projected + offsets[None, :]], axis=1)


def factor_gram(features):
    gram = lax.dot_general(features, features, (((0,), (0,)), ((), ())), precision=HIGHEST,
                           preferred_element_type=jnp.float32)
    gram = gram + RIDGE_TERM * jnp.eye(BASIS, dtype=jnp.float32)
    half = BASIS // 2
    identity = jnp.eye(half, dtype=jnp.float32)
    upper_factor = jnp.linalg.cholesky(gram[:half, :half])
    upper_inverse = lax.linalg.triangular_solve(upper_factor, identity, left_side=True, lower=True)
    below = lax.dot_general(gram[half:, :half], upper_inverse, (((1,), (1,)), ((), ())), precision=HIGHEST,
                            preferred_element_type=jnp.float32)
    rest = gram[half:, half:] - lax.dot_general(below, below, (((1,), (1,)), ((), ())), precision=HIGHEST,
                                                preferred_element_type=jnp.float32)
    lower_factor = jnp.linalg.cholesky(rest)
    lower_inverse = lax.linalg.triangular_solve(lower_factor, identity, left_side=True, lower=True)
    return upper_inverse, below, lower_inverse


def matvec(matrix, vector, transpose=False):
    dims = (((0,), (0,)), ((), ())) if transpose else (((1,), (0,)), ((), ()))
    return lax.dot_general(matrix, vector, dims, precision=HIGHEST, preferred_element_type=jnp.float32)


def solve_weights(factor, features, values):
    upper_inverse, below, lower_inverse = factor
    half = BASIS // 2
    right_side = lax.dot_general(features, values, (((0,), (0,)), ((), ())), precision=HIGHEST,
                                 preferred_element_type=jnp.float32)
    first = matvec(upper_inverse, right_side[:half])
    second = matvec(lower_inverse, right_side[half:] - matvec(below, first))
    second = matvec(lower_inverse, second, transpose=True)
    first = matvec(upper_inverse, first - matvec(below, second, transpose=True), transpose=True)
    return jnp.concatenate([first, second])


def new_values(weights, current, quad_dirs, offsets):
    moments = moments_of(current, quad_dirs, offsets)
    carried = jnp.dot(moments, weights, precision=HIGHEST, preferred_element_type=jnp.float32)
    return jnp.maximum(exercise_rows(current), DISCOUNT * carried)


def go_home(owner_values, weights, slots, rank, owners, reps):
    width = BASIS // reps
    dates = len(owner_values)
    per_home = [jnp.broadcast_to(v.reshape(owners, 1, MOST), (owners, reps, MOST)) for v in owner_values]
    blocks = [jnp.broadcast_to(w.reshape(1, reps, width), (owners, reps, width)) for w in weights]
    message = jnp.concatenate(per_home + blocks, axis=2).reshape(owners * reps, dates * (MOST + width))
    arrived = lax.all_to_all(message, ("path", "rep"), 0, 0, tiled=True)
    values = []
    for d in range(dates):
        by_slot = arrived[:, d * MOST:(d + 1) * MOST]
        picked = lax.dot_general(by_slot, slots[d], (((0,), (0,)), ((), ())), precision=HIGHEST,
                                 preferred_element_type=jnp.float32)
        ranks = lax.broadcasted_iota(jnp.int32, picked.shape, 0)
        values.append(jnp.sum(jnp.where(ranks == rank[d][None, :], picked, 0.0), axis=0))
    mine = lax.dynamic_index_in_dim(arrived.reshape(owners, reps, -1), lax.axis_index("path"), 0, False)
    mine = mine[:, dates * MOST:]
    return values, [mine[:, d * width:(d + 1) * width] for d in range(dates)]


def body(start_state, increments, vol_factor, quad_dirs, bundle_ids, bundle_slot):
    reps = lax.axis_size("rep")
    owners = bundle_slot.shape[0] // reps
    rep_index = lax.axis_index("rep")
    middle = start_state + jnp.dot(
        vol_factor, increments[0], precision=HIGHEST, preferred_element_type=jnp.float32
    )
    final = middle + jnp.dot(
        vol_factor, increments[1], precision=HIGHEST, preferred_element_type=jnp.float32
    )
    mixed = jnp.dot(quad_dirs, vol_factor, precision=HIGHEST, preferred_element_type=jnp.float32)
    offsets = jnp.sum(mixed * mixed, axis=1)
    assets = start_state.shape[0]
    ones = jnp.ones((1, start_state.shape[1]), jnp.float32)

    late_map, late_slots, late_rank, late_slot_of = routing(bundle_ids[0, :, 0], bundle_slot, rep_index, reps)
    early_map, early_slots, early_rank, _ = routing(bundle_ids[1, :, 0], bundle_slot, rep_index, reps)

    late_label = late_slot_of.astype(jnp.float32)[None, :]
    outgoing = jnp.concatenate(
        [send_rows(late_map, jnp.concatenate([ones, middle, final], axis=0)),
         send_rows(early_map, jnp.concatenate([ones, start_state, middle, late_label], axis=0))], axis=1)
    arrived = exchange(outgoing, owners)
    width = 1 + 2 * assets

    late_rows = arrived[:, :width]
    present = late_rows[:, :1]
    current = late_rows[:, 1:1 + assets]
    following = late_rows[:, 1 + assets:]
    late_features = features_of(present, following, quad_dirs)
    late_factor = factor_gram(late_features)
    late_weights = solve_weights(late_factor, late_features, exercise_rows(following))
    late_owner_values = new_values(late_weights, current, quad_dirs, offsets)
    copies = jnp.broadcast_to(late_weights[None, :], (owners * reps, BASIS))
    late_table = lax.all_to_all(copies, ("path", "rep"), 0, 0, tiled=True)

    early_rows = arrived[:, width:]
    present = early_rows[:, :1]
    current = early_rows[:, 1:1 + assets]
    following = early_rows[:, 1 + assets:1 + 2 * assets]
    late_slot_here = early_rows[:, 1 + 2 * assets].astype(jnp.int32)
    early_features = features_of(present, following, quad_dirs)
    early_factor = factor_gram(early_features)
    table_rows = lax.broadcasted_iota(jnp.int32, (late_slot_here.shape[0], late_table.shape[0]), 1)
    chooser = (table_rows == late_slot_here[:, None]).astype(jnp.float32)
    chosen = jnp.dot(chooser, late_table, precision=HIGHEST, preferred_element_type=jnp.float32)
    moments = moments_of(following, quad_dirs, offsets)
    carried = jnp.sum(moments * chosen, axis=1)
    early_targets = jnp.maximum(exercise_rows(following), DISCOUNT * carried)
    early_weights = solve_weights(early_factor, early_features, early_targets)
    early_owner_values = new_values(early_weights, current, quad_dirs, offsets)

    (value_middle, value_start), (late_block, early_block) = go_home(
        [late_owner_values, early_owner_values], [late_weights, early_weights],
        [late_slots, early_slots], [late_rank, early_rank], owners, reps)
    return (jnp.stack([value_middle, value_start]), jnp.stack([late_block, early_block]))


def solution(mesh):
    placed = (P(None, "path"), P(None, None, "path"), P(), P(), P(None, "path", None), P())
    return jax.shard_map(
        body,
        mesh=mesh,
        in_specs=placed,
        out_specs=(P(None, "path"), P(None, "path", "rep")),
        check_vma=False,
    )
```

```python
import jax
import jax.numpy as jnp
from jax import lax
from jax.sharding import PartitionSpec as P

BASIS = 256
MOST = 8

RIDGE_TERM = 32.0
DISCOUNT = 0.97
NOTIONAL = 10.0
HIGHEST = lax.Precision.HIGHEST


def exercise_value(states):
    return NOTIONAL * jnp.maximum(jnp.mean(jnp.exp(states), axis=0) - 1.0, 0.0)


def exercise_rows(states):
    return NOTIONAL * jnp.maximum(jnp.mean(jnp.exp(states), axis=1) - 1.0, 0.0)


def routing(bundle_of, bundle_slot, rep_index, reps):
    path_count = bundle_of.shape[0]
    bundles = bundle_slot.shape[0]
    labels = lax.broadcasted_iota(jnp.int32, (path_count, bundles), 1)
    slot_of = jnp.sum(jnp.where(bundle_of[:, None] == labels, bundle_slot[None, :], 0), axis=1)
    owners = bundles // reps
    later = lax.broadcasted_iota(jnp.int32, (path_count, path_count), 0)
    earlier = lax.broadcasted_iota(jnp.int32, (path_count, path_count), 1)
    same = (slot_of[:, None] == slot_of[None, :]) & (earlier < later)
    rank = jnp.sum(same.astype(jnp.int32), axis=1)
    mine = (slot_of % reps) == rep_index
    position = jnp.where(mine, (slot_of // reps) * MOST + rank, -1)
    places = lax.broadcasted_iota(jnp.int32, (owners * MOST, path_count), 0)
    forward = (places == position[None, :]).astype(jnp.float32)
    slot_rows = lax.broadcasted_iota(jnp.int32, (bundles, path_count), 0)
    slots = (slot_rows == slot_of[None, :]).astype(jnp.float32)
    return forward, slots, rank, slot_of


def send_rows(onehot, rows):
    return lax.dot_general(onehot, rows, (((1,), (1,)), ((), ())), precision=HIGHEST,
                           preferred_element_type=jnp.float32)


def exchange(block, owners):
    shaped = block.reshape((owners, MOST) + block.shape[1:])
    arrived = lax.all_to_all(shaped, "path", 0, 0, tiled=True)
    return arrived.reshape(block.shape)


def features_of(present, states, quad_dirs):
    projected = lax.dot_general(states, quad_dirs, (((1,), (1,)), ((), ())), precision=HIGHEST,
                                preferred_element_type=jnp.float32)
    return jnp.concatenate([present, states, projected * projected], axis=1)


def moments_of(states, quad_dirs, offsets):
    projected = lax.dot_general(states, quad_dirs, (((1,), (1,)), ((), ())), precision=HIGHEST,
                                preferred_element_type=jnp.float32)
    constant = jnp.ones((states.shape[0], 1), jnp.float32)
    return jnp.concatenate([constant, states, projected * projected + offsets[None, :]], axis=1)


def factor_gram(features):
    gram = lax.dot_general(features, features, (((0,), (0,)), ((), ())), precision=HIGHEST,
                           preferred_element_type=jnp.float32)
    gram = gram + RIDGE_TERM * jnp.eye(BASIS, dtype=jnp.float32)
    half = BASIS // 2
    identity = jnp.eye(half, dtype=jnp.float32)
    side = gram[half:, :half]
    corner = gram[half:, half:]

    def step(index, carry):
        block, inverses, below = carry
        factor = jnp.linalg.cholesky(block)
        inverse = lax.linalg.triangular_solve(factor, identity, left_side=True, lower=True)
        inverses = lax.dynamic_update_index_in_dim(inverses, inverse, index, 0)
        below = jnp.where(index == 0, lax.dot_general(side, inverse, (((1,), (1,)), ((), ())), precision=HIGHEST,
                                                      preferred_element_type=jnp.float32), below)
        block = corner - lax.dot_general(below, below, (((1,), (1,)), ((), ())), precision=HIGHEST,
                                         preferred_element_type=jnp.float32)
        return block, inverses, below

    start = (gram[:half, :half], jnp.zeros((2, half, half), jnp.float32), jnp.zeros((half, half), jnp.float32))
    _, inverses, below = lax.fori_loop(0, 2, step, start)
    return inverses[0], below, inverses[1]


def matvec(matrix, vector, transpose=False):
    dims = (((0,), (0,)), ((), ())) if transpose else (((1,), (0,)), ((), ()))
    return lax.dot_general(matrix, vector, dims, precision=HIGHEST, preferred_element_type=jnp.float32)


def solve_weights(factor, features, values):
    upper_inverse, below, lower_inverse = factor
    half = BASIS // 2
    right_side = lax.dot_general(features, values, (((0,), (0,)), ((), ())), precision=HIGHEST,
                                 preferred_element_type=jnp.float32)
    first = matvec(upper_inverse, right_side[:half])
    second = matvec(lower_inverse, right_side[half:] - matvec(below, first))
    second = matvec(lower_inverse, second, transpose=True)
    first = matvec(upper_inverse, first - matvec(below, second, transpose=True), transpose=True)
    return jnp.concatenate([first, second])


def new_values(weights, current, quad_dirs, offsets):
    moments = moments_of(current, quad_dirs, offsets)
    carried = jnp.dot(moments, weights, precision=HIGHEST, preferred_element_type=jnp.float32)
    return jnp.maximum(exercise_rows(current), DISCOUNT * carried)


def go_home(owner_values, weights, slots, rank, owners, reps):
    width = BASIS // reps
    dates = len(owner_values)
    per_home = [jnp.broadcast_to(v.reshape(owners, 1, MOST), (owners, reps, MOST)) for v in owner_values]
    blocks = jnp.broadcast_to(weights.reshape(1, reps, width), (owners, reps, width))
    message = jnp.concatenate(per_home + [blocks], axis=2).reshape(owners * reps, dates * MOST + width)
    arrived = lax.all_to_all(message, ("path", "rep"), 0, 0, tiled=True)
    values = []
    for d in range(dates):
        by_slot = arrived[:, d * MOST:(d + 1) * MOST]
        picked = lax.dot_general(by_slot, slots[d], (((0,), (0,)), ((), ())), precision=HIGHEST,
                                 preferred_element_type=jnp.float32)
        ranks = lax.broadcasted_iota(jnp.int32, picked.shape, 0)
        values.append(jnp.sum(jnp.where(ranks == rank[d][None, :], picked, 0.0), axis=0))
    mine = lax.dynamic_index_in_dim(arrived.reshape(owners, reps, -1), lax.axis_index("path"), 0, False)
    return values, mine[:, dates * MOST:]


def body(start_state, increments, vol_factor, quad_dirs, bundle_ids, bundle_slot):
    reps = lax.axis_size("rep")
    owners = bundle_slot.shape[0] // reps
    rep_index = lax.axis_index("rep")
    middle = start_state + jnp.dot(
        vol_factor, increments[0], precision=HIGHEST, preferred_element_type=jnp.float32
    )
    final = middle + jnp.dot(
        vol_factor, increments[1], precision=HIGHEST, preferred_element_type=jnp.float32
    )
    mixed = jnp.dot(quad_dirs, vol_factor, precision=HIGHEST, preferred_element_type=jnp.float32)
    offsets = jnp.sum(mixed * mixed, axis=1)
    assets = start_state.shape[0]
    ones = jnp.ones((1, start_state.shape[1]), jnp.float32)

    late_map, late_slots, late_rank, late_slot_of = routing(bundle_ids[0, :, 0], bundle_slot, rep_index, reps)
    early_map, early_slots, early_rank, _ = routing(bundle_ids[1, :, 0], bundle_slot, rep_index, reps)

    late_label = late_slot_of.astype(jnp.float32)[None, :]
    outgoing = jnp.concatenate(
        [send_rows(late_map, jnp.concatenate([ones, middle, final], axis=0)),
         send_rows(early_map, jnp.concatenate([ones, start_state, middle, late_label], axis=0))], axis=1)
    arrived = exchange(outgoing, owners)
    width = 1 + 2 * assets

    late_rows = arrived[:, :width]
    present = late_rows[:, :1]
    current = late_rows[:, 1:1 + assets]
    following = late_rows[:, 1 + assets:]
    late_features = features_of(present, following, quad_dirs)
    late_factor = factor_gram(late_features)
    late_weights = solve_weights(late_factor, late_features, exercise_rows(following))
    late_owner_values = new_values(late_weights, current, quad_dirs, offsets)
    copies = jnp.broadcast_to(late_weights[None, :], (owners * reps, BASIS))
    late_table = lax.all_to_all(copies, ("path", "rep"), 0, 0, tiled=True)

    early_rows = arrived[:, width:]
    present = early_rows[:, :1]
    current = early_rows[:, 1:1 + assets]
    following = early_rows[:, 1 + assets:1 + 2 * assets]
    late_slot_here = early_rows[:, 1 + 2 * assets].astype(jnp.int32)
    early_features = features_of(present, following, quad_dirs)
    early_factor = factor_gram(early_features)
    table_rows = lax.broadcasted_iota(jnp.int32, (late_slot_here.shape[0], late_table.shape[0]), 1)
    chooser = (table_rows == late_slot_here[:, None]).astype(jnp.float32)
    chosen = jnp.dot(chooser, late_table, precision=HIGHEST, preferred_element_type=jnp.float32)
    moments = moments_of(following, quad_dirs, offsets)
    carried = jnp.sum(moments * chosen, axis=1)
    early_targets = jnp.maximum(exercise_rows(following), DISCOUNT * carried)
    early_weights = solve_weights(early_factor, early_features, early_targets)
    early_owner_values = new_values(early_weights, current, quad_dirs, offsets)

    (value_middle, value_start), early_block = go_home(
        [late_owner_values, early_owner_values], early_weights,
        [late_slots, early_slots], [late_rank, early_rank], owners, reps)
    width = BASIS // reps
    late_block = lax.dynamic_slice(
        late_table, (lax.axis_index("path") * reps, rep_index * width), (reps, width))
    return (jnp.stack([value_middle, value_start]), jnp.stack([late_block, early_block]))


def solution(mesh):
    placed = (P(None, "path"), P(None, None, "path"), P(), P(), P(None, "path", None), P())
    return jax.shard_map(
        body,
        mesh=mesh,
        in_specs=placed,
        out_specs=(P(None, "path"), P(None, "path", "rep")),
        check_vma=False,
    )
```

```python
import jax
import jax.numpy as jnp
from jax import lax
from jax.sharding import PartitionSpec as P

BASIS = 256
MOST = 8

RIDGE_TERM = 32.0
DISCOUNT = 0.97
NOTIONAL = 10.0
HIGHEST = lax.Precision.HIGHEST


def exercise_value(states):
    return NOTIONAL * jnp.maximum(jnp.mean(jnp.exp(states), axis=0) - 1.0, 0.0)


def exercise_rows(states):
    return NOTIONAL * jnp.maximum(jnp.mean(jnp.exp(states), axis=1) - 1.0, 0.0)


def routing(bundle_of, bundle_slot, rep_index, reps):
    path_count = bundle_of.shape[0]
    bundles = bundle_slot.shape[0]
    labels = lax.broadcasted_iota(jnp.int32, (path_count, bundles), 1)
    slot_of = jnp.sum(jnp.where(bundle_of[:, None] == labels, bundle_slot[None, :], 0), axis=1)
    owners = bundles // reps
    later = lax.broadcasted_iota(jnp.int32, (path_count, path_count), 0)
    earlier = lax.broadcasted_iota(jnp.int32, (path_count, path_count), 1)
    same = (slot_of[:, None] == slot_of[None, :]) & (earlier < later)
    rank = jnp.sum(same.astype(jnp.int32), axis=1)
    mine = (slot_of % reps) == rep_index
    position = jnp.where(mine, (slot_of // reps) * MOST + rank, -1)
    places = lax.broadcasted_iota(jnp.int32, (owners * MOST, path_count), 0)
    forward = (places == position[None, :]).astype(jnp.float32)
    slot_rows = lax.broadcasted_iota(jnp.int32, (bundles, path_count), 0)
    slots = (slot_rows == slot_of[None, :]).astype(jnp.float32)
    return forward, slots, rank, slot_of


def send_rows(onehot, rows):
    return lax.dot_general(onehot, rows, (((1,), (1,)), ((), ())), precision=HIGHEST,
                           preferred_element_type=jnp.float32)


def exchange(block, owners):
    shaped = block.reshape(owners, -1)
    arrived = lax.all_to_all(shaped, "path", 0, 0, tiled=True)
    return arrived.reshape(block.shape)


def features_of(present, states, quad_dirs):
    projected = lax.dot_general(states, quad_dirs, (((1,), (1,)), ((), ())), precision=HIGHEST,
                                preferred_element_type=jnp.float32)
    return jnp.concatenate([present, states, projected * projected], axis=1)


def moments_of(states, quad_dirs, offsets):
    projected = lax.dot_general(states, quad_dirs, (((1,), (1,)), ((), ())), precision=HIGHEST,
                                preferred_element_type=jnp.float32)
    constant = jnp.ones((states.shape[0], 1), jnp.float32)
    return jnp.concatenate([constant, states, projected * projected + offsets[None, :]], axis=1)


def factor_gram(features):
    gram = lax.dot_general(features, features, (((0,), (0,)), ((), ())), precision=HIGHEST,
                           preferred_element_type=jnp.float32)
    gram = gram + RIDGE_TERM * jnp.eye(BASIS, dtype=jnp.float32)
    half = BASIS // 2
    identity = jnp.eye(half, dtype=jnp.float32)
    side = gram[half:, :half]
    corner = gram[half:, half:]

    def step(index, carry):
        block, inverses, below = carry
        factor = jnp.linalg.cholesky(block)
        inverse = lax.linalg.triangular_solve(factor, identity, left_side=True, lower=True)
        inverses = lax.dynamic_update_index_in_dim(inverses, inverse, index, 0)
        below = jnp.where(index == 0, lax.dot_general(side, inverse, (((1,), (1,)), ((), ())), precision=HIGHEST,
                                                      preferred_element_type=jnp.float32), below)
        block = corner - lax.dot_general(below, below, (((1,), (1,)), ((), ())), precision=HIGHEST,
                                         preferred_element_type=jnp.float32)
        return block, inverses, below

    start = (gram[:half, :half], jnp.zeros((2, half, half), jnp.float32), jnp.zeros((half, half), jnp.float32))
    _, inverses, below = lax.fori_loop(0, 2, step, start)
    return inverses[0], below, inverses[1]


def matvec(matrix, vector, transpose=False):
    dims = (((0,), (0,)), ((), ())) if transpose else (((1,), (0,)), ((), ()))
    return lax.dot_general(matrix, vector, dims, precision=HIGHEST, preferred_element_type=jnp.float32)


def solve_weights(factor, features, values):
    upper_inverse, below, lower_inverse = factor
    half = BASIS // 2
    right_side = lax.dot_general(features, values, (((0,), (0,)), ((), ())), precision=HIGHEST,
                                 preferred_element_type=jnp.float32)
    first = matvec(upper_inverse, right_side[:half])
    second = matvec(lower_inverse, right_side[half:] - matvec(below, first))
    second = matvec(lower_inverse, second, transpose=True)
    first = matvec(upper_inverse, first - matvec(below, second, transpose=True), transpose=True)
    return jnp.concatenate([first, second])


def new_values(weights, current, quad_dirs, offsets):
    moments = moments_of(current, quad_dirs, offsets)
    carried = jnp.dot(moments, weights, precision=HIGHEST, preferred_element_type=jnp.float32)
    return jnp.maximum(exercise_rows(current), DISCOUNT * carried)


def go_home(owner_values, weights, slots, rank, owners, reps):
    width = BASIS // reps
    dates = len(owner_values)
    per_home = [jnp.broadcast_to(v.reshape(owners, 1, MOST), (owners, reps, MOST)) for v in owner_values]
    blocks = jnp.broadcast_to(weights.reshape(1, reps, width), (owners, reps, width))
    message = jnp.concatenate(per_home + [blocks], axis=2).reshape(owners * reps, dates * MOST + width)
    arrived = lax.all_to_all(message, ("path", "rep"), 0, 0, tiled=True)
    values = []
    for d in range(dates):
        by_slot = arrived[:, d * MOST:(d + 1) * MOST]
        picked = lax.dot_general(by_slot, slots[d], (((0,), (0,)), ((), ())), precision=HIGHEST,
                                 preferred_element_type=jnp.float32)
        ranks = lax.broadcasted_iota(jnp.int32, picked.shape, 0)
        values.append(jnp.sum(jnp.where(ranks == rank[d][None, :], picked, 0.0), axis=0))
    mine = lax.dynamic_index_in_dim(arrived.reshape(owners, reps, -1), lax.axis_index("path"), 0, False)
    return values, mine[:, dates * MOST:]


def body(start_state, increments, vol_factor, quad_dirs, bundle_ids, bundle_slot):
    reps = lax.axis_size("rep")
    owners = bundle_slot.shape[0] // reps
    rep_index = lax.axis_index("rep")
    middle = start_state + jnp.dot(
        vol_factor, increments[0], precision=HIGHEST, preferred_element_type=jnp.float32
    )
    final = middle + jnp.dot(
        vol_factor, increments[1], precision=HIGHEST, preferred_element_type=jnp.float32
    )
    mixed = jnp.dot(quad_dirs, vol_factor, precision=HIGHEST, preferred_element_type=jnp.float32)
    offsets = jnp.sum(mixed * mixed, axis=1)
    assets = start_state.shape[0]
    ones = jnp.ones((1, start_state.shape[1]), jnp.float32)

    late_map, late_slots, late_rank, late_slot_of = routing(bundle_ids[0, :, 0], bundle_slot, rep_index, reps)
    early_map, early_slots, early_rank, _ = routing(bundle_ids[1, :, 0], bundle_slot, rep_index, reps)

    late_label = late_slot_of.astype(jnp.float32)[None, :]
    outgoing = jnp.concatenate(
        [send_rows(late_map, jnp.concatenate([ones, middle, final], axis=0)),
         send_rows(early_map, jnp.concatenate([ones, start_state, middle, late_label], axis=0))], axis=1)
    arrived = exchange(outgoing, owners)
    width = 1 + 2 * assets

    late_rows = arrived[:, :width]
    present = late_rows[:, :1]
    current = late_rows[:, 1:1 + assets]
    following = late_rows[:, 1 + assets:]
    late_features = features_of(present, following, quad_dirs)
    late_factor = factor_gram(late_features)
    late_weights = solve_weights(late_factor, late_features, exercise_rows(following))
    late_owner_values = new_values(late_weights, current, quad_dirs, offsets)
    copies = jnp.broadcast_to(late_weights[None, :], (owners * reps, BASIS))
    late_table = lax.all_to_all(copies, ("path", "rep"), 0, 0, tiled=True)

    early_rows = arrived[:, width:]
    present = early_rows[:, :1]
    current = early_rows[:, 1:1 + assets]
    following = early_rows[:, 1 + assets:1 + 2 * assets]
    late_slot_here = early_rows[:, 1 + 2 * assets].astype(jnp.int32)
    early_features = features_of(present, following, quad_dirs)
    early_factor = factor_gram(early_features)
    table_rows = lax.broadcasted_iota(jnp.int32, (late_slot_here.shape[0], late_table.shape[0]), 1)
    chooser = (table_rows == late_slot_here[:, None]).astype(jnp.float32)
    chosen = jnp.dot(chooser, late_table, precision=HIGHEST, preferred_element_type=jnp.float32)
    moments = moments_of(following, quad_dirs, offsets)
    carried = jnp.sum(moments * chosen, axis=1)
    early_targets = jnp.maximum(exercise_rows(following), DISCOUNT * carried)
    early_weights = solve_weights(early_factor, early_features, early_targets)
    early_owner_values = new_values(early_weights, current, quad_dirs, offsets)

    (value_middle, value_start), early_block = go_home(
        [late_owner_values, early_owner_values], early_weights,
        [late_slots, early_slots], [late_rank, early_rank], owners, reps)
    width = BASIS // reps
    late_block = lax.dynamic_slice(
        late_table, (lax.axis_index("path") * reps, rep_index * width), (reps, width))
    return (jnp.stack([value_middle, value_start]), jnp.stack([late_block, early_block]))


def solution(mesh):
    placed = (P(None, "path"), P(None, None, "path"), P(), P(), P(None, "path", None), P())
    return jax.shard_map(
        body,
        mesh=mesh,
        in_specs=placed,
        out_specs=(P(None, "path"), P(None, "path", "rep")),
        check_vma=False,
    )
```

```python
import jax
import jax.numpy as jnp
from jax import lax
from jax.sharding import PartitionSpec as P

BASIS = 256
MOST = 8

RIDGE_TERM = 32.0
DISCOUNT = 0.97
NOTIONAL = 10.0
HIGHEST = lax.Precision.HIGHEST


def exercise_value(states):
    return NOTIONAL * jnp.maximum(jnp.mean(jnp.exp(states), axis=0) - 1.0, 0.0)


def exercise_rows(states):
    return NOTIONAL * jnp.maximum(jnp.mean(jnp.exp(states), axis=1) - 1.0, 0.0)


def routing(bundle_of, bundle_slot, rep_index, reps):
    path_count = bundle_of.shape[0]
    bundles = bundle_slot.shape[0]
    labels = lax.broadcasted_iota(jnp.int32, (path_count, bundles), 1)
    slot_of = jnp.sum(jnp.where(bundle_of[:, None] == labels, bundle_slot[None, :], 0), axis=1)
    owners = bundles // reps
    block = 128
    blocks = path_count // block
    hot = (slot_of[:, None] == lax.broadcasted_iota(jnp.int32, (path_count, bundles), 1)).astype(jnp.bfloat16)
    hot = hot.reshape(blocks, block, bundles)
    within = (lax.broadcasted_iota(jnp.int32, (block, block), 1)
              < lax.broadcasted_iota(jnp.int32, (block, block), 0)).astype(jnp.bfloat16)
    counts = jnp.einsum("pq,bqs->bps", within, hot, preferred_element_type=jnp.float32)
    totals = jnp.sum(hot.astype(jnp.float32), axis=1)
    before = (lax.broadcasted_iota(jnp.int32, (blocks, blocks), 1)
              < lax.broadcasted_iota(jnp.int32, (blocks, blocks), 0)).astype(jnp.float32)
    offsets_by_block = jnp.dot(before, totals, precision=HIGHEST, preferred_element_type=jnp.float32)
    counts = counts + offsets_by_block[:, None, :]
    rank = jnp.sum(counts * hot.astype(jnp.float32), axis=2).reshape(path_count).astype(jnp.int32)
    mine = (slot_of % reps) == rep_index
    position = jnp.where(mine, (slot_of // reps) * MOST + rank, -1)
    places = lax.broadcasted_iota(jnp.int32, (owners * MOST, path_count), 0)
    forward = (places == position[None, :]).astype(jnp.float32)
    slot_rows = lax.broadcasted_iota(jnp.int32, (bundles, path_count), 0)
    slots = (slot_rows == slot_of[None, :]).astype(jnp.float32)
    return forward, slots, rank, slot_of


def send_rows(onehot, rows):
    return lax.dot_general(onehot, rows, (((1,), (1,)), ((), ())), precision=HIGHEST,
                           preferred_element_type=jnp.float32)


def exchange(block, owners):
    shaped = block.reshape(owners, -1)
    arrived = lax.all_to_all(shaped, "path", 0, 0, tiled=True)
    return arrived.reshape(block.shape)


def features_of(present, states, quad_dirs):
    projected = lax.dot_general(states, quad_dirs, (((1,), (1,)), ((), ())), precision=HIGHEST,
                                preferred_element_type=jnp.float32)
    return jnp.concatenate([present, states, projected * projected], axis=1)


def moments_of(states, quad_dirs, offsets):
    projected = lax.dot_general(states, quad_dirs, (((1,), (1,)), ((), ())), precision=HIGHEST,
                                preferred_element_type=jnp.float32)
    constant = jnp.ones((states.shape[0], 1), jnp.float32)
    return jnp.concatenate([constant, states, projected * projected + offsets[None, :]], axis=1)


def factor_gram(features):
    gram = lax.dot_general(features, features, (((0,), (0,)), ((), ())), precision=HIGHEST,
                           preferred_element_type=jnp.float32)
    gram = gram + RIDGE_TERM * jnp.eye(BASIS, dtype=jnp.float32)
    half = BASIS // 2
    identity = jnp.eye(half, dtype=jnp.float32)
    side = gram[half:, :half]
    corner = gram[half:, half:]

    def step(index, carry):
        block, inverses, below = carry
        factor = jnp.linalg.cholesky(block)
        inverse = lax.linalg.triangular_solve(factor, identity, left_side=True, lower=True)
        inverses = lax.dynamic_update_index_in_dim(inverses, inverse, index, 0)
        below = jnp.where(index == 0, lax.dot_general(side, inverse, (((1,), (1,)), ((), ())), precision=HIGHEST,
                                                      preferred_element_type=jnp.float32), below)
        block = corner - lax.dot_general(below, below, (((1,), (1,)), ((), ())), precision=HIGHEST,
                                         preferred_element_type=jnp.float32)
        return block, inverses, below

    start = (gram[:half, :half], jnp.zeros((2, half, half), jnp.float32), jnp.zeros((half, half), jnp.float32))
    _, inverses, below = lax.fori_loop(0, 2, step, start)
    return inverses[0], below, inverses[1]


def matvec(matrix, vector, transpose=False):
    dims = (((0,), (0,)), ((), ())) if transpose else (((1,), (0,)), ((), ()))
    return lax.dot_general(matrix, vector, dims, precision=HIGHEST, preferred_element_type=jnp.float32)


def solve_weights(factor, features, values):
    upper_inverse, below, lower_inverse = factor
    half = BASIS // 2
    right_side = lax.dot_general(features, values, (((0,), (0,)), ((), ())), precision=HIGHEST,
                                 preferred_element_type=jnp.float32)
    first = matvec(upper_inverse, right_side[:half])
    second = matvec(lower_inverse, right_side[half:] - matvec(below, first))
    second = matvec(lower_inverse, second, transpose=True)
    first = matvec(upper_inverse, first - matvec(below, second, transpose=True), transpose=True)
    return jnp.concatenate([first, second])


def new_values(weights, current, quad_dirs, offsets):
    moments = moments_of(current, quad_dirs, offsets)
    carried = jnp.dot(moments, weights, precision=HIGHEST, preferred_element_type=jnp.float32)
    return jnp.maximum(exercise_rows(current), DISCOUNT * carried)


def go_home(owner_values, weights, slots, rank, owners, reps):
    width = BASIS // reps
    dates = len(owner_values)
    per_home = [jnp.broadcast_to(v.reshape(owners, 1, MOST), (owners, reps, MOST)) for v in owner_values]
    blocks = jnp.broadcast_to(weights.reshape(1, reps, width), (owners, reps, width))
    message = jnp.concatenate(per_home + [blocks], axis=2).reshape(owners * reps, dates * MOST + width)
    arrived = lax.all_to_all(message, ("path", "rep"), 0, 0, tiled=True)
    values = []
    for d in range(dates):
        by_slot = arrived[:, d * MOST:(d + 1) * MOST]
        picked = lax.dot_general(by_slot, slots[d], (((0,), (0,)), ((), ())), precision=HIGHEST,
                                 preferred_element_type=jnp.float32)
        ranks = lax.broadcasted_iota(jnp.int32, picked.shape, 0)
        values.append(jnp.sum(jnp.where(ranks == rank[d][None, :], picked, 0.0), axis=0))
    mine = lax.dynamic_index_in_dim(arrived.reshape(owners, reps, -1), lax.axis_index("path"), 0, False)
    return values, mine[:, dates * MOST:]


def body(start_state, increments, vol_factor, quad_dirs, bundle_ids, bundle_slot):
    reps = lax.axis_size("rep")
    owners = bundle_slot.shape[0] // reps
    rep_index = lax.axis_index("rep")
    middle = start_state + jnp.dot(
        vol_factor, increments[0], precision=HIGHEST, preferred_element_type=jnp.float32
    )
    final = middle + jnp.dot(
        vol_factor, increments[1], precision=HIGHEST, preferred_element_type=jnp.float32
    )
    mixed = jnp.dot(quad_dirs, vol_factor, precision=HIGHEST, preferred_element_type=jnp.float32)
    offsets = jnp.sum(mixed * mixed, axis=1)
    assets = start_state.shape[0]
    ones = jnp.ones((1, start_state.shape[1]), jnp.float32)

    late_map, late_slots, late_rank, late_slot_of = routing(bundle_ids[0, :, 0], bundle_slot, rep_index, reps)
    early_map, early_slots, early_rank, _ = routing(bundle_ids[1, :, 0], bundle_slot, rep_index, reps)

    late_label = late_slot_of.astype(jnp.float32)[None, :]
    outgoing = jnp.concatenate(
        [send_rows(late_map, jnp.concatenate([ones, middle, final], axis=0)),
         send_rows(early_map, jnp.concatenate([ones, start_state, middle, late_label], axis=0))], axis=1)
    arrived = exchange(outgoing, owners)
    width = 1 + 2 * assets

    late_rows = arrived[:, :width]
    present = late_rows[:, :1]
    current = late_rows[:, 1:1 + assets]
    following = late_rows[:, 1 + assets:]
    late_features = features_of(present, following, quad_dirs)
    late_factor = factor_gram(late_features)
    late_weights = solve_weights(late_factor, late_features, exercise_rows(following))
    late_owner_values = new_values(late_weights, current, quad_dirs, offsets)
    copies = jnp.broadcast_to(late_weights[None, :], (owners * reps, BASIS))
    late_table = lax.all_to_all(copies, ("path", "rep"), 0, 0, tiled=True)

    early_rows = arrived[:, width:]
    present = early_rows[:, :1]
    current = early_rows[:, 1:1 + assets]
    following = early_rows[:, 1 + assets:1 + 2 * assets]
    late_slot_here = early_rows[:, 1 + 2 * assets].astype(jnp.int32)
    early_features = features_of(present, following, quad_dirs)
    early_factor = factor_gram(early_features)
    table_rows = lax.broadcasted_iota(jnp.int32, (late_slot_here.shape[0], late_table.shape[0]), 1)
    chooser = (table_rows == late_slot_here[:, None]).astype(jnp.float32)
    chosen = jnp.dot(chooser, late_table, precision=HIGHEST, preferred_element_type=jnp.float32)
    moments = moments_of(following, quad_dirs, offsets)
    carried = jnp.sum(moments * chosen, axis=1)
    early_targets = jnp.maximum(exercise_rows(following), DISCOUNT * carried)
    early_weights = solve_weights(early_factor, early_features, early_targets)
    early_owner_values = new_values(early_weights, current, quad_dirs, offsets)

    (value_middle, value_start), early_block = go_home(
        [late_owner_values, early_owner_values], early_weights,
        [late_slots, early_slots], [late_rank, early_rank], owners, reps)
    width = BASIS // reps
    late_block = lax.dynamic_slice(
        late_table, (lax.axis_index("path") * reps, rep_index * width), (reps, width))
    return (jnp.stack([value_middle, value_start]), jnp.stack([late_block, early_block]))


def solution(mesh):
    placed = (P(None, "path"), P(None, None, "path"), P(), P(), P(None, "path", None), P())
    return jax.shard_map(
        body,
        mesh=mesh,
        in_specs=placed,
        out_specs=(P(None, "path"), P(None, "path", "rep")),
        check_vma=False,
    )
```
